128 devices in a mesh: gx: 8 (over x, core), yz: 16 (over z, y).
Axes of the slice: x: 4, y: 4, z: 4, core: 2. Of those that a mesh axis runs over, the one named last changes fastest.
Arguments:
- hidden_in: bfloat16 [2, 128, 8192], P(None, ('gx', 'yz')), may hold values from -6 to 6
- k_cache: bfloat16 [128, 1024, 1024], P(('gx', 'yz'))
- v_cache: bfloat16 [128, 1024, 1024], P(('gx', 'yz')), may hold values from -6 to 6
- lengths: int32 [128], P(('gx', 'yz')), may hold values from 1 to 1024, as said below
- counts: int32 [128, 16], P(('gx', 'yz')), may hold values from 0 to 3
- token_elem: int32 [512], replicated, may hold values from 0 to 16, as said below
- tokens: int32 [128], P(('gx', 'yz')), may hold values from 0 to 511
- attn_gain: float32 [8192], replicated, may hold values from 0.5 to 1.5
- qkv_weight: bfloat16 [8192, 10240], P('gx', 'yz'), may hold values from -0.0625 to 0.0625
- o_weight: bfloat16 [8192, 8192], P('gx', 'yz'), may hold values from -0.0625 to 0.0625
- ffn_gain: float32 [8192], replicated, may hold values from 0.5 to 1.5
- gate_up_weight: bfloat16 [8192, 57344], P('gx', 'yz'), may hold values from -0.0625 to 0.0625
- down_weight: bfloat16 [28672, 8192], P('gx', 'yz'), may hold values from -0.03125 to 0.03125
- final_gain: float32 [8192], replicated, may hold values from 0.5 to 1.5
- lm_weight: bfloat16 [8192, 512], P(('gx', 'yz'))
Outputs:
- layer_out: bfloat16 [2, 128, 8192], P(None, ('gx', 'yz'))
- log_probs: float32 [2, 128, 512], P(None, ('gx', 'yz'))
The draws below stay inside these ranges and needn't reach their ends.
Inputs may be any that keep to these rules, and one draw needn't show every extreme that they name: `lengths`: some spectrum uses all 1024 positions. `token_elem`: some token has no element (value 16).
All inputs are finite; a program needn't handle non-finite values.
Results may differ from the reference program's by a relative error of at most 0.022.
Values may be sent and summed in bfloat16 or wider, within the bound.
No kernel may reach another device: no remote copies, remote signals or barrier semaphores. Data moves between devices by JAX's collectives and lax.ppermute only.
A program may use at most 128 MiB of HBM per device.

```python
import math
import jax
import jax.numpy as jnp
from jax import lax

D = 8192
FF = 28672
HEADS = 64
KV_HEADS = 8
HEAD = 128
VOCAB = 512
ELEMENTS = 16
CACHE = 1024
BATCH = 128


def draw_k_cache(key, part):
    base_key = jax.random.fold_in(key, 0)
    values = jax.random.normal(base_key, (BATCH, CACHE, KV_HEADS * HEAD), jnp.float32)
    return values.astype(jnp.bfloat16)


def draw_lm_weight(key, part):
    base_key = jax.random.fold_in(key, 0)
    values = jax.random.normal(base_key, (D, VOCAB), jnp.float32) * (3.0 / math.sqrt(D))
    return values.astype(jnp.bfloat16)


def draw_lengths(key, part):
    base_key, pick_key = jax.random.split(key)
    drawn = jax.random.randint(base_key, (BATCH,), 1, CACHE + 1)
    target = jax.random.randint(pick_key, (), 0, BATCH)
    return drawn.at[target].set(CACHE).astype(jnp.int32)


def draw_token_elem(key, part):
    base_key, pick_key = jax.random.split(key)
    drawn = jax.random.randint(base_key, (VOCAB,), 0, ELEMENTS + 1)
    target = jax.random.randint(pick_key, (), 0, VOCAB)
    return drawn.at[target].set(ELEMENTS).astype(jnp.int32)


def plant(array, key, least, high):
    longest = array.shape.index(max(array.shape))
    spots = []
    for shift in (0, 1):
        where = [jax.random.randint(jax.random.fold_in(key, axis), (), 0, length) for axis, length in enumerate(array.shape)]
        where[longest] = (where[longest] + shift) % array.shape[longest]
        spots.append(tuple(where))
    return array.at[spots[0]].set(least).at[spots[1]].set(high)


def block_levels(key, dims, cuts, smallest, high):
    def one(dim, blocks):
        draws = jax.random.uniform(jax.random.fold_in(jax.random.fold_in(key, 6), dim), (blocks,), jnp.float32, smallest / len(cuts), high / len(cuts))
        return jnp.repeat(jnp.exp(draws), dims[dim] // blocks).reshape((-1,) + (1,) * (len(dims) - dim - 1))

    level = one(*cuts[0])
    for cut in cuts[1:]:
        level = level * one(*cut)
    return level


def bell_draw(rng, shape, scale, bound, cuts=(), held_as=jnp.bfloat16):
    array = scale * jax.random.normal(rng, shape, jnp.float32)
    if cuts:
        array = array * block_levels(rng, shape, cuts, -0.22, 0.18)
    return jnp.clip(array, -bound, bound).astype(held_as)


def setup_inputs(seed: int = 0) -> dict:
    splits = jax.random.split(jax.random.key(seed), 16)
    return {
        "hidden_in": bell_draw(splits[0], (2, BATCH, D), 1.0, 6.0, ((1, 128),)),
        "k_cache": draw_k_cache(jax.random.fold_in(splits[15], 71), 0),
        "v_cache": bell_draw(splits[2], (BATCH, CACHE, KV_HEADS * HEAD), 1.0, 6.0, ((0, 128),)),
        "lengths": draw_lengths(jax.random.fold_in(splits[15], 71), 0),
        "counts": plant(jax.random.randint(splits[4], (BATCH, ELEMENTS), 0, 4), jax.random.fold_in(splits[4], 1), 0, 3).astype(jnp.int32),
        "token_elem": draw_token_elem(jax.random.fold_in(splits[15], 71), 0),
        "tokens": plant(jax.random.randint(splits[6], (BATCH,), 0, VOCAB), jax.random.fold_in(splits[6], 1), 0, VOCAB - 1).astype(jnp.int32),
        "attn_gain": jnp.clip(1.0 + 0.1 * jax.random.normal(splits[7], (D,), jnp.float32), 0.5, 1.5),
        "qkv_weight": bell_draw(splits[8], (D, D + 2 * KV_HEADS * HEAD), D ** -0.5, 0.0625, ((0, 8), (1, 16))),
        "o_weight": bell_draw(splits[9], (HEADS * HEAD, D), (HEADS * HEAD) ** -0.5, 0.0625, ((0, 8), (1, 16))),
        "ffn_gain": jnp.clip(1.0 + 0.1 * jax.random.normal(splits[10], (D,), jnp.float32), 0.5, 1.5),
        "gate_up_weight": bell_draw(splits[11], (D, 2 * FF), D ** -0.5, 0.0625, ((0, 8), (1, 16))),
        "down_weight": bell_draw(splits[12], (FF, D), FF ** -0.5, 0.03125, ((0, 8), (1, 16))),
        "final_gain": jnp.clip(1.0 + 0.1 * jax.random.normal(splits[13], (D,), jnp.float32), 0.5, 1.5),
        "lm_weight": draw_lm_weight(jax.random.fold_in(splits[15], 71), 0),
    }


NORM_EPS = 1e-05
ROPE_THETA = 500000.0

def norm_rows(values, gain_vec):
    wide = values.astype(jnp.float32)
    inverse = lax.rsqrt(lax.optimization_barrier(jnp.mean(wide * wide, axis=-1, keepdims=True)) + NORM_EPS)
    return (wide * inverse * gain_vec.astype(jnp.float32)).astype(jnp.bfloat16)

def rotate(heads_in, positions):
    half_width = heads_in.shape[-1] // 2
    frequency = jnp.power(ROPE_THETA, -(jnp.arange(half_width, dtype=jnp.float32) * 2.0 / heads_in.shape[-1]))
    angles = positions.astype(jnp.float32)[:, None] * frequency[None, :]
    cos_part = jnp.cos(angles)[:, None, :]
    sin_part = jnp.sin(angles)[:, None, :]
    wide = heads_in.astype(jnp.float32)
    first_half = wide[..., :half_width]
    second_half = wide[..., half_width:]
    joined = jnp.concatenate([first_half * cos_part - second_half * sin_part, second_half * cos_part + first_half * sin_part], -1)
    return joined.astype(jnp.bfloat16)

def attention(queries, k_cache, v_cache, lengths, keys_new, values_new):
    groups = HEADS // KV_HEADS
    factor = 1.0 / math.sqrt(HEAD)

    def per_row(row_items):
        query_row, kcache_row, vcache_row, length_row, knew_row, vnew_row = row_items
        query_wide = query_row.astype(jnp.float32).reshape(KV_HEADS, groups, HEAD)
        kcache_wide = kcache_row.astype(jnp.float32).reshape(CACHE, KV_HEADS, HEAD)
        vcache_wide = vcache_row.astype(jnp.float32).reshape(CACHE, KV_HEADS, HEAD)
        scores_cache = jnp.einsum('kgd,lkd->kgl', query_wide, kcache_wide) * factor
        valid = (jnp.arange(CACHE) < length_row)[None, None, :]
        scores_cache = jnp.where(valid, scores_cache, -jnp.inf)
        scores_new = jnp.einsum('kgd,nkd->kgn', query_wide, knew_row.astype(jnp.float32)) * factor
        largest = jnp.maximum(lax.optimization_barrier(jnp.max(scores_cache, -1)), lax.optimization_barrier(jnp.max(scores_new, -1)))[..., None]
        exp_cache = jnp.where(valid, jnp.exp(scores_cache - largest), 0.0)
        exp_new = jnp.exp(scores_new - largest)
        denominator = lax.optimization_barrier(jnp.sum(exp_cache, -1, keepdims=True)) + lax.optimization_barrier(jnp.sum(exp_new, -1, keepdims=True))
        weights_cache = (exp_cache / denominator).astype(jnp.bfloat16)
        weights_new = (exp_new / denominator).astype(jnp.bfloat16)
        result = jnp.einsum('kgl,lkd->kgd', weights_cache.astype(jnp.float32), vcache_wide)
        result = result + jnp.einsum('kgn,nkd->kgd', weights_new.astype(jnp.float32), vnew_row.astype(jnp.float32))
        return result.reshape(HEADS * HEAD).astype(jnp.bfloat16)
    return lax.map(per_row, (queries, k_cache, v_cache, lengths, keys_new, values_new))

def element_table(token_elem):
    return (token_elem[:, None] == jnp.arange(ELEMENTS, dtype=jnp.int32)[None, :]).astype(jnp.float32)

def masked_log_probs(logits, remaining, token_elem):
    element_hot = element_table(token_elem)
    per_token = jnp.dot(remaining, element_hot.T)
    allowed = (per_token > 0.5) | (token_elem == ELEMENTS)[None, :]
    largest = lax.optimization_barrier(jnp.max(jnp.where(allowed, logits, -jnp.inf), -1, keepdims=True))
    shifted = logits - largest
    denominator = lax.optimization_barrier(jnp.sum(jnp.where(allowed, jnp.exp(shifted), 0.0), -1, keepdims=True))
    return jnp.where(allowed, shifted - jnp.log(denominator), 0.0)

def used_elements(tokens, token_elem):
    token_hot = (tokens[:, None] == jnp.arange(VOCAB, dtype=jnp.int32)[None, :]).astype(jnp.float32)
    return jnp.dot(token_hot, element_table(token_elem))

def reference(hidden_in, k_cache, v_cache, lengths, counts, token_elem, tokens, attn_gain, qkv_weight, o_weight, ffn_gain, gate_up_weight, down_weight, final_gain, lm_weight):
    q_width = HEADS * HEAD
    kv_width = KV_HEADS * HEAD
    key_list = []
    value_list = []
    result_list = []
    log_list = []
    remaining = counts.astype(jnp.float32)
    for which_step in range(2):
        layer_in = hidden_in[which_step]
        normed = norm_rows(layer_in, attn_gain)
        mixed = jnp.dot(normed, qkv_weight, preferred_element_type=jnp.float32).astype(jnp.bfloat16)
        positions = lengths + which_step
        queries = rotate(mixed[:, :q_width].reshape(BATCH, HEADS, HEAD), positions)
        keys_now = rotate(mixed[:, q_width:q_width + kv_width].reshape(BATCH, KV_HEADS, HEAD), positions)
        values_now = mixed[:, q_width + kv_width:].reshape(BATCH, KV_HEADS, HEAD)
        key_list.append(keys_now)
        value_list.append(values_now)
        attended = attention(queries, k_cache, v_cache, lengths, jnp.stack(key_list, 1), jnp.stack(value_list, 1))
        projected = jnp.dot(attended, o_weight, preferred_element_type=jnp.float32).astype(jnp.bfloat16)
        residual = (layer_in.astype(jnp.float32) + projected.astype(jnp.float32)).astype(jnp.bfloat16)
        gate_up = jnp.dot(norm_rows(residual, ffn_gain), gate_up_weight, preferred_element_type=jnp.float32).astype(jnp.bfloat16)
        hidden_units = (jax.nn.silu(gate_up[:, :FF].astype(jnp.float32)) * gate_up[:, FF:].astype(jnp.float32)).astype(jnp.bfloat16)
        lowered = jnp.dot(hidden_units, down_weight, preferred_element_type=jnp.float32).astype(jnp.bfloat16)
        result = (residual.astype(jnp.float32) + lowered.astype(jnp.float32)).astype(jnp.bfloat16)
        logits = jnp.dot(norm_rows(result, final_gain), lm_weight, preferred_element_type=jnp.float32)
        log_list.append(masked_log_probs(logits, remaining, token_elem))
        result_list.append(result)
        remaining = remaining - used_elements(tokens, token_elem)
    return (jnp.stack(result_list), jnp.stack(log_list))
```

```python
import math

import jax
import jax.numpy as jnp
from jax import lax
from jax.sharding import PartitionSpec as P

FF = 28672
HEADS = 64
KV_HEADS = 8
HEAD = 128
VOCAB = 512
ELEMENTS = 16


NORM_EPS = 1e-05
ROPE_THETA = 500000.0


def norm_rows(values, gain_vec):
    wide = values.astype(jnp.float32)
    inverse = lax.rsqrt(jnp.mean(wide * wide, axis=-1, keepdims=True) + NORM_EPS)
    return (wide * inverse * gain_vec).astype(jnp.bfloat16)


def rotate(heads_in, positions):
    half_width = heads_in.shape[-1] // 2
    frequency = jnp.power(
        ROPE_THETA, -(jnp.arange(half_width, dtype=jnp.float32) * 2.0 / heads_in.shape[-1])
    )
    angles = positions.astype(jnp.float32)[:, None] * frequency[None, :]
    cos_part = jnp.cos(angles)[:, None, :]
    sin_part = jnp.sin(angles)[:, None, :]
    wide = heads_in.astype(jnp.float32)
    first_half = wide[..., :half_width]
    second_half = wide[..., half_width:]
    joined = jnp.concatenate(
        [
            first_half * cos_part - second_half * sin_part,
            second_half * cos_part + first_half * sin_part,
        ],
        -1,
    )
    return joined.astype(jnp.bfloat16)


def spread_rows(inputs):
    gathered = lax.all_gather(inputs, "yz", axis=0, tiled=True)
    return lax.all_to_all(gathered, "gx", split_axis=1, concat_axis=0, tiled=True)


def project(inputs, weight):
    spread = spread_rows(inputs)
    summed = lax.psum_scatter(
        jnp.dot(spread, weight, preferred_element_type=jnp.float32),
        "gx",
        scatter_dimension=0,
        tiled=True,
    )
    return lax.all_to_all(
        summed.astype(jnp.bfloat16), "yz", split_axis=0, concat_axis=1, tiled=True
    )


def head_logits(normed, lm_weight):
    slice_width = lm_weight.shape[0]
    offset_cols = lax.axis_index("yz") * slice_width
    spread = spread_rows(normed)
    own_cols = lax.dynamic_slice_in_dim(spread, offset_cols, slice_width, 1)
    return lax.psum_scatter(
        jnp.dot(own_cols, lm_weight, preferred_element_type=jnp.float32),
        ("gx", "yz"),
        scatter_dimension=0,
        tiled=True,
    )


def attend(queries, k_cache, v_cache, lengths, keys_new, values_new):
    groups = HEADS // KV_HEADS
    factor = 1.0 / math.sqrt(HEAD)
    steps = queries.shape[0]
    cache_len = k_cache.shape[1]
    query_heads = queries.reshape(steps, KV_HEADS, groups, HEAD)
    kcache_heads = k_cache.reshape(cache_len, KV_HEADS, HEAD)
    vcache_heads = v_cache.reshape(cache_len, KV_HEADS, HEAD)
    knew_heads = keys_new.reshape(steps, KV_HEADS, HEAD)
    vnew_heads = values_new.reshape(steps, KV_HEADS, HEAD)
    scores_cache = (
        jnp.einsum("skgd,lkd->skgl", query_heads, kcache_heads, preferred_element_type=jnp.float32)
        * factor
    )
    valid = jnp.arange(cache_len)[None, None, None, :] < lengths[0]
    scores_cache = jnp.where(valid, scores_cache, -jnp.inf)
    scores_new = (
        jnp.einsum("skgd,nkd->skgn", query_heads, knew_heads, preferred_element_type=jnp.float32)
        * factor
    )
    causal = (
        jnp.arange(steps)[None, None, None, :] <= jnp.arange(steps)[:, None, None, None]
    )
    scores_new = jnp.where(causal, scores_new, -jnp.inf)
    largest = jnp.maximum(jnp.max(scores_cache, -1), jnp.max(scores_new, -1))[..., None]
    exp_cache = jnp.where(valid, jnp.exp(scores_cache - largest), 0.0)
    exp_new = jnp.where(causal, jnp.exp(scores_new - largest), 0.0)
    denominator = jnp.sum(exp_cache, -1, keepdims=True) + jnp.sum(exp_new, -1, keepdims=True)
    weights_cache = (exp_cache / denominator).astype(jnp.bfloat16)
    weights_new = (exp_new / denominator).astype(jnp.bfloat16)
    result = jnp.einsum(
        "skgl,lkd->skgd", weights_cache, vcache_heads, preferred_element_type=jnp.float32
    )
    result = result + jnp.einsum(
        "skgn,nkd->skgd", weights_new, vnew_heads, preferred_element_type=jnp.float32
    )
    return result.reshape(steps, HEADS * HEAD).astype(jnp.bfloat16)


def element_table(token_elem):
    return (token_elem[:, None] == jnp.arange(ELEMENTS, dtype=jnp.int32)[None, :]).astype(
        jnp.float32
    )


def masked_log_probs(logits, remaining, token_elem):
    element_hot = element_table(token_elem)
    per_token = jnp.dot(remaining, element_hot.T)
    allowed = (per_token > 0.5) | (token_elem == ELEMENTS)[None, :]
    largest = jnp.max(jnp.where(allowed, logits, -jnp.inf), -1, keepdims=True)
    shifted = logits - largest
    denominator = jnp.sum(jnp.where(allowed, jnp.exp(shifted), 0.0), -1, keepdims=True)
    return jnp.where(allowed, shifted - jnp.log(denominator), 0.0)


def used_elements(tokens, token_elem):
    token_hot = (tokens[:, None] == jnp.arange(VOCAB, dtype=jnp.int32)[None, :]).astype(jnp.float32)
    return jnp.dot(token_hot, element_table(token_elem))


def per_device(
    hidden_in,
    k_cache,
    v_cache,
    lengths,
    counts,
    token_elem,
    tokens,
    attn_gain,
    qkv_weight,
    o_weight,
    ffn_gain,
    gate_up_weight,
    down_weight,
    final_gain,
    lm_weight,
):
    q_width = HEADS * HEAD
    kv_width = KV_HEADS * HEAD
    steps = hidden_in.shape[0]
    layer_in = hidden_in[:, 0, :]
    positions = lengths[0] + jnp.arange(steps, dtype=jnp.int32)
    mixed = project(norm_rows(layer_in, attn_gain), qkv_weight)
    queries = rotate(mixed[:, :q_width].reshape(-1, HEADS, HEAD), positions).reshape(-1, q_width)
    keys_now = rotate(
        mixed[:, q_width : q_width + kv_width].reshape(-1, KV_HEADS, HEAD), positions
    ).reshape(-1, kv_width)
    values_now = mixed[:, q_width + kv_width :]
    attended = attend(queries, k_cache[0], v_cache[0], lengths, keys_now, values_now)
    projected = project(attended, o_weight)
    residual = (layer_in.astype(jnp.float32) + projected.astype(jnp.float32)).astype(jnp.bfloat16)
    gate_up = project(norm_rows(residual, ffn_gain), gate_up_weight)
    hidden_units = (
        jax.nn.silu(gate_up[:, :FF].astype(jnp.float32)) * gate_up[:, FF:].astype(jnp.float32)
    ).astype(jnp.bfloat16)
    lowered = project(hidden_units, down_weight)
    result = (residual.astype(jnp.float32) + lowered.astype(jnp.float32)).astype(jnp.bfloat16)
    logits = head_logits(norm_rows(result, final_gain), lm_weight)
    remaining = counts.astype(jnp.float32)
    first_log = masked_log_probs(logits[0:1], remaining, token_elem)
    remaining = remaining - used_elements(tokens, token_elem)
    second_log = masked_log_probs(logits[1:2], remaining, token_elem)
    return (result[:, None, :], jnp.stack([first_log, second_log]))


def solution(mesh):
    return jax.shard_map(
        per_device,
        mesh=mesh,
        in_specs=(
            P(None, ("gx", "yz"), None),
            P(("gx", "yz"), None, None),
            P(("gx", "yz"), None, None),
            P(("gx", "yz")),
            P(("gx", "yz"), None),
            P(),
            P(("gx", "yz")),
            P(),
            P("gx", "yz"),
            P("gx", "yz"),
            P(),
            P("gx", "yz"),
            P("gx", "yz"),
            P(),
            P(("gx", "yz"), None),
        ),
        out_specs=(P(None, ("gx", "yz"), None), P(None, ("gx", "yz"), None)),
        check_vma=False,
    )
```

```python
import math

import jax
import jax.numpy as jnp
from jax import lax
from jax.sharding import PartitionSpec as P

FF = 28672
HEADS = 64
KV_HEADS = 8
HEAD = 128
VOCAB = 512
ELEMENTS = 16


NORM_EPS = 1e-05
ROPE_THETA = 500000.0


def norm_rows(values, gain_vec):
    wide = values.astype(jnp.float32)
    inverse = lax.rsqrt(jnp.mean(wide * wide, axis=-1, keepdims=True) + NORM_EPS)
    return (wide * inverse * gain_vec).astype(jnp.bfloat16)


def rotate(heads_in, positions):
    half_width = heads_in.shape[-1] // 2
    frequency = jnp.power(
        ROPE_THETA, -(jnp.arange(half_width, dtype=jnp.float32) * 2.0 / heads_in.shape[-1])
    )
    angles = positions.astype(jnp.float32)[:, None] * frequency[None, :]
    cos_part = jnp.cos(angles)[:, None, :]
    sin_part = jnp.sin(angles)[:, None, :]
    wide = heads_in.astype(jnp.float32)
    first_half = wide[..., :half_width]
    second_half = wide[..., half_width:]
    joined = jnp.concatenate(
        [
            first_half * cos_part - second_half * sin_part,
            second_half * cos_part + first_half * sin_part,
        ],
        -1,
    )
    return joined.astype(jnp.bfloat16)


ALL = ("gx", "yz")


def spread_rows(inputs, groups):
    rows_here, width = inputs.shape
    block = width // groups
    blocks = inputs.reshape(rows_here, groups, block).transpose(1, 0, 2)
    devices = lax.psum(1, ALL)
    send = jnp.broadcast_to(
        blocks[:, None], (groups, devices // groups, rows_here, block)
    ).reshape(devices, rows_here, block)
    got = lax.all_to_all(send, ALL, 0, 0, tiled=True)
    return got.reshape(devices * rows_here, block)


def gather_rows(partial, groups):
    rows, width = partial.shape
    devices = lax.psum(1, ALL)
    rows_here = rows // devices
    got = lax.all_to_all(partial.reshape(devices, rows_here, width), ALL, 0, 0, tiled=True)
    summed = jnp.sum(got.reshape(groups, devices // groups, rows_here, width), axis=0)
    return summed.transpose(1, 0, 2).reshape(rows_here, (devices // groups) * width)


def project(inputs, weight):
    groups = lax.psum(1, "gx")
    spread = spread_rows(inputs, groups)
    partial = jnp.dot(spread, weight, preferred_element_type=jnp.float32)
    return gather_rows(partial, groups).astype(jnp.bfloat16)


def head_logits(normed, lm_full):
    return jnp.dot(normed, lm_full, preferred_element_type=jnp.float32)


def attend(queries, k_cache, v_cache, lengths, keys_new, values_new):
    groups = HEADS // KV_HEADS
    factor = 1.0 / math.sqrt(HEAD)
    steps = queries.shape[0]
    cache_len = k_cache.shape[1]
    query_heads = queries.reshape(steps, KV_HEADS, groups, HEAD)
    kcache_heads = k_cache.reshape(cache_len, KV_HEADS, HEAD)
    vcache_heads = v_cache.reshape(cache_len, KV_HEADS, HEAD)
    knew_heads = keys_new.reshape(steps, KV_HEADS, HEAD)
    vnew_heads = values_new.reshape(steps, KV_HEADS, HEAD)
    scores_cache = (
        jnp.einsum("skgd,lkd->skgl", query_heads, kcache_heads, preferred_element_type=jnp.float32)
        * factor
    )
    valid = jnp.arange(cache_len)[None, None, None, :] < lengths[0]
    scores_cache = jnp.where(valid, scores_cache, -jnp.inf)
    scores_new = (
        jnp.einsum("skgd,nkd->skgn", query_heads, knew_heads, preferred_element_type=jnp.float32)
        * factor
    )
    causal = (
        jnp.arange(steps)[None, None, None, :] <= jnp.arange(steps)[:, None, None, None]
    )
    scores_new = jnp.where(causal, scores_new, -jnp.inf)
    largest = jnp.maximum(jnp.max(scores_cache, -1), jnp.max(scores_new, -1))[..., None]
    exp_cache = jnp.where(valid, jnp.exp(scores_cache - largest), 0.0)
    exp_new = jnp.where(causal, jnp.exp(scores_new - largest), 0.0)
    denominator = jnp.sum(exp_cache, -1, keepdims=True) + jnp.sum(exp_new, -1, keepdims=True)
    weights_cache = (exp_cache / denominator).astype(jnp.bfloat16)
    weights_new = (exp_new / denominator).astype(jnp.bfloat16)
    result = jnp.einsum(
        "skgl,lkd->skgd", weights_cache, vcache_heads, preferred_element_type=jnp.float32
    )
    result = result + jnp.einsum(
        "skgn,nkd->skgd", weights_new, vnew_heads, preferred_element_type=jnp.float32
    )
    return result.reshape(steps, HEADS * HEAD).astype(jnp.bfloat16)


def element_table(token_elem):
    return (token_elem[:, None] == jnp.arange(ELEMENTS, dtype=jnp.int32)[None, :]).astype(
        jnp.float32
    )


def masked_log_probs(logits, remaining, token_elem):
    element_hot = element_table(token_elem)
    per_token = jnp.dot(remaining, element_hot.T)
    allowed = (per_token > 0.5) | (token_elem == ELEMENTS)[None, :]
    largest = jnp.max(jnp.where(allowed, logits, -jnp.inf), -1, keepdims=True)
    shifted = logits - largest
    denominator = jnp.sum(jnp.where(allowed, jnp.exp(shifted), 0.0), -1, keepdims=True)
    return jnp.where(allowed, shifted - jnp.log(denominator), 0.0)


def used_elements(tokens, token_elem):
    token_hot = (tokens[:, None] == jnp.arange(VOCAB, dtype=jnp.int32)[None, :]).astype(jnp.float32)
    return jnp.dot(token_hot, element_table(token_elem))


def per_device(
    hidden_in,
    k_cache,
    v_cache,
    lengths,
    counts,
    token_elem,
    tokens,
    attn_gain,
    qkv_weight,
    o_weight,
    ffn_gain,
    gate_up_weight,
    down_weight,
    final_gain,
    lm_weight,
):
    q_width = HEADS * HEAD
    kv_width = KV_HEADS * HEAD
    steps = hidden_in.shape[0]
    lm_full = lax.all_gather(lm_weight, ALL, axis=0, tiled=True)
    layer_in = hidden_in[:, 0, :]
    positions = lengths[0] + jnp.arange(steps, dtype=jnp.int32)
    mixed = project(norm_rows(layer_in, attn_gain), qkv_weight)
    queries = rotate(mixed[:, :q_width].reshape(-1, HEADS, HEAD), positions).reshape(-1, q_width)
    keys_now = rotate(
        mixed[:, q_width : q_width + kv_width].reshape(-1, KV_HEADS, HEAD), positions
    ).reshape(-1, kv_width)
    values_now = mixed[:, q_width + kv_width :]
    attended = attend(queries, k_cache[0], v_cache[0], lengths, keys_now, values_now)
    projected = project(attended, o_weight)
    residual = (layer_in.astype(jnp.float32) + projected.astype(jnp.float32)).astype(jnp.bfloat16)
    gate_up = project(norm_rows(residual, ffn_gain), gate_up_weight)
    hidden_units = (
        jax.nn.silu(gate_up[:, :FF].astype(jnp.float32)) * gate_up[:, FF:].astype(jnp.float32)
    ).astype(jnp.bfloat16)
    lowered = project(hidden_units, down_weight)
    result = (residual.astype(jnp.float32) + lowered.astype(jnp.float32)).astype(jnp.bfloat16)
    logits = head_logits(norm_rows(result, final_gain), lm_full)
    remaining = counts.astype(jnp.float32)
    first_log = masked_log_probs(logits[0:1], remaining, token_elem)
    remaining = remaining - used_elements(tokens, token_elem)
    second_log = masked_log_probs(logits[1:2], remaining, token_elem)
    return (result[:, None, :], jnp.stack([first_log, second_log]))


def solution(mesh):
    return jax.shard_map(
        per_device,
        mesh=mesh,
        in_specs=(
            P(None, ("gx", "yz"), None),
            P(("gx", "yz"), None, None),
            P(("gx", "yz"), None, None),
            P(("gx", "yz")),
            P(("gx", "yz"), None),
            P(),
            P(("gx", "yz")),
            P(),
            P("gx", "yz"),
            P("gx", "yz"),
            P(),
            P("gx", "yz"),
            P("gx", "yz"),
            P(),
            P(("gx", "yz"), None),
        ),
        out_specs=(P(None, ("gx", "yz"), None), P(None, ("gx", "yz"), None)),
        check_vma=False,
    )
```

```python
import math

import jax
import jax.numpy as jnp
from jax import lax
from jax.sharding import PartitionSpec as P

FF = 28672
HEADS = 64
KV_HEADS = 8
HEAD = 128
VOCAB = 512
ELEMENTS = 16


NORM_EPS = 1e-05
ROPE_THETA = 500000.0


def norm_rows(values, gain_vec):
    wide = values.astype(jnp.float32)
    inverse = lax.rsqrt(jnp.mean(wide * wide, axis=-1, keepdims=True) + NORM_EPS)
    return (wide * inverse * gain_vec).astype(jnp.bfloat16)


def rotate(heads_in, positions):
    half_width = heads_in.shape[-1] // 2
    frequency = jnp.power(
        ROPE_THETA, -(jnp.arange(half_width, dtype=jnp.float32) * 2.0 / heads_in.shape[-1])
    )
    angles = positions.astype(jnp.float32)[:, None] * frequency[None, :]
    cos_part = jnp.cos(angles)[:, None, :]
    sin_part = jnp.sin(angles)[:, None, :]
    wide = heads_in.astype(jnp.float32)
    first_half = wide[..., :half_width]
    second_half = wide[..., half_width:]
    joined = jnp.concatenate(
        [
            first_half * cos_part - second_half * sin_part,
            second_half * cos_part + first_half * sin_part,
        ],
        -1,
    )
    return joined.astype(jnp.bfloat16)


ALL = ("gx", "yz")


def spread_rows(inputs, groups):
    rows_here, width = inputs.shape
    block = width // groups
    blocks = inputs.reshape(rows_here, groups, block).transpose(1, 0, 2)
    devices = lax.psum(1, ALL)
    send = jnp.broadcast_to(
        blocks[:, None], (groups, devices // groups, rows_here, block)
    ).reshape(devices, rows_here, block)
    got = lax.all_to_all(send, ALL, 0, 0, tiled=True)
    return got.reshape(devices * rows_here, block)


def gather_rows(partial, groups, link_type=jnp.float32):
    rows, width = partial.shape
    partial = partial.astype(link_type)
    devices = lax.psum(1, ALL)
    rows_here = rows // devices
    got = lax.all_to_all(partial.reshape(devices, rows_here, width), ALL, 0, 0, tiled=True)
    summed = jnp.sum(
        got.reshape(groups, devices // groups, rows_here, width).astype(jnp.float32), axis=0
    )
    return summed.transpose(1, 0, 2).reshape(rows_here, (devices // groups) * width)


def project(inputs, weight, link_type=jnp.float32):
    groups = lax.psum(1, "gx")
    spread = spread_rows(inputs, groups)
    partial = jnp.dot(spread, weight, preferred_element_type=jnp.float32)
    return gather_rows(partial, groups, link_type).astype(jnp.bfloat16)


def head_logits(normed, lm_full):
    return jnp.dot(normed, lm_full, preferred_element_type=jnp.float32)


def attend(queries, k_cache, v_cache, lengths, keys_new, values_new):
    groups = HEADS // KV_HEADS
    factor = 1.0 / math.sqrt(HEAD)
    steps = queries.shape[0]
    cache_len = k_cache.shape[1]
    query_heads = queries.reshape(steps, KV_HEADS, groups, HEAD)
    kcache_heads = k_cache.reshape(cache_len, KV_HEADS, HEAD)
    vcache_heads = v_cache.reshape(cache_len, KV_HEADS, HEAD)
    knew_heads = keys_new.reshape(steps, KV_HEADS, HEAD)
    vnew_heads = values_new.reshape(steps, KV_HEADS, HEAD)
    scores_cache = (
        jnp.einsum("skgd,lkd->skgl", query_heads, kcache_heads, preferred_element_type=jnp.float32)
        * factor
    )
    valid = jnp.arange(cache_len)[None, None, None, :] < lengths[0]
    scores_cache = jnp.where(valid, scores_cache, -jnp.inf)
    scores_new = (
        jnp.einsum("skgd,nkd->skgn", query_heads, knew_heads, preferred_element_type=jnp.float32)
        * factor
    )
    causal = (
        jnp.arange(steps)[None, None, None, :] <= jnp.arange(steps)[:, None, None, None]
    )
    scores_new = jnp.where(causal, scores_new, -jnp.inf)
    largest = jnp.maximum(jnp.max(scores_cache, -1), jnp.max(scores_new, -1))[..., None]
    exp_cache = jnp.where(valid, jnp.exp(scores_cache - largest), 0.0)
    exp_new = jnp.where(causal, jnp.exp(scores_new - largest), 0.0)
    denominator = jnp.sum(exp_cache, -1, keepdims=True) + jnp.sum(exp_new, -1, keepdims=True)
    weights_cache = (exp_cache / denominator).astype(jnp.bfloat16)
    weights_new = (exp_new / denominator).astype(jnp.bfloat16)
    result = jnp.einsum(
        "skgl,lkd->skgd", weights_cache, vcache_heads, preferred_element_type=jnp.float32
    )
    result = result + jnp.einsum(
        "skgn,nkd->skgd", weights_new, vnew_heads, preferred_element_type=jnp.float32
    )
    return result.reshape(steps, HEADS * HEAD).astype(jnp.bfloat16)


def element_table(token_elem):
    return (token_elem[:, None] == jnp.arange(ELEMENTS, dtype=jnp.int32)[None, :]).astype(
        jnp.float32
    )


def masked_log_probs(logits, remaining, token_elem):
    element_hot = element_table(token_elem)
    per_token = jnp.dot(remaining, element_hot.T)
    allowed = (per_token > 0.5) | (token_elem == ELEMENTS)[None, :]
    largest = jnp.max(jnp.where(allowed, logits, -jnp.inf), -1, keepdims=True)
    shifted = logits - largest
    denominator = jnp.sum(jnp.where(allowed, jnp.exp(shifted), 0.0), -1, keepdims=True)
    return jnp.where(allowed, shifted - jnp.log(denominator), 0.0)


def used_elements(tokens, token_elem):
    token_hot = (tokens[:, None] == jnp.arange(VOCAB, dtype=jnp.int32)[None, :]).astype(jnp.float32)
    return jnp.dot(token_hot, element_table(token_elem))


def per_device(
    hidden_in,
    k_cache,
    v_cache,
    lengths,
    counts,
    token_elem,
    tokens,
    attn_gain,
    qkv_weight,
    o_weight,
    ffn_gain,
    gate_up_weight,
    down_weight,
    final_gain,
    lm_weight,
):
    q_width = HEADS * HEAD
    kv_width = KV_HEADS * HEAD
    steps = hidden_in.shape[0]
    lm_full = lax.all_gather(lm_weight, ALL, axis=0, tiled=True)
    layer_in = hidden_in[:, 0, :]
    positions = lengths[0] + jnp.arange(steps, dtype=jnp.int32)
    mixed = project(norm_rows(layer_in, attn_gain), qkv_weight)
    queries = rotate(mixed[:, :q_width].reshape(-1, HEADS, HEAD), positions).reshape(-1, q_width)
    keys_now = rotate(
        mixed[:, q_width : q_width + kv_width].reshape(-1, KV_HEADS, HEAD), positions
    ).reshape(-1, kv_width)
    values_now = mixed[:, q_width + kv_width :]
    attended = attend(queries, k_cache[0], v_cache[0], lengths, keys_now, values_now)
    projected = project(attended, o_weight)
    residual = (layer_in.astype(jnp.float32) + projected.astype(jnp.float32)).astype(jnp.bfloat16)
    gate_up = project(norm_rows(residual, ffn_gain), gate_up_weight, jnp.bfloat16)
    hidden_units = (
        jax.nn.silu(gate_up[:, :FF].astype(jnp.float32)) * gate_up[:, FF:].astype(jnp.float32)
    ).astype(jnp.bfloat16)
    lowered = project(hidden_units, down_weight)
    result = (residual.astype(jnp.float32) + lowered.astype(jnp.float32)).astype(jnp.bfloat16)
    logits = head_logits(norm_rows(result, final_gain), lm_full)
    remaining = counts.astype(jnp.float32)
    first_log = masked_log_probs(logits[0:1], remaining, token_elem)
    remaining = remaining - used_elements(tokens, token_elem)
    second_log = masked_log_probs(logits[1:2], remaining, token_elem)
    return (result[:, None, :], jnp.stack([first_log, second_log]))


def solution(mesh):
    return jax.shard_map(
        per_device,
        mesh=mesh,
        in_specs=(
            P(None, ("gx", "yz"), None),
            P(("gx", "yz"), None, None),
            P(("gx", "yz"), None, None),
            P(("gx", "yz")),
            P(("gx", "yz"), None),
            P(),
            P(("gx", "yz")),
            P(),
            P("gx", "yz"),
            P("gx", "yz"),
            P(),
            P("gx", "yz"),
            P("gx", "yz"),
            P(),
            P(("gx", "yz"), None),
        ),
        out_specs=(P(None, ("gx", "yz"), None), P(None, ("gx", "yz"), None)),
        check_vma=False,
    )
```

```python
import math

import jax
import jax.numpy as jnp
from jax import lax
from jax.sharding import PartitionSpec as P

FF = 28672
HEADS = 64
KV_HEADS = 8
HEAD = 128
VOCAB = 512
ELEMENTS = 16


NORM_EPS = 1e-05
ROPE_THETA = 500000.0


def norm_rows(values, gain_vec):
    wide = values.astype(jnp.float32)
    inverse = lax.rsqrt(jnp.mean(wide * wide, axis=-1, keepdims=True) + NORM_EPS)
    return (wide * inverse * gain_vec).astype(jnp.bfloat16)


def rotate(heads_in, positions):
    half_width = heads_in.shape[-1] // 2
    frequency = jnp.power(
        ROPE_THETA, -(jnp.arange(half_width, dtype=jnp.float32) * 2.0 / heads_in.shape[-1])
    )
    angles = positions.astype(jnp.float32)[:, None] * frequency[None, :]
    cos_part = jnp.cos(angles)[:, None, :]
    sin_part = jnp.sin(angles)[:, None, :]
    wide = heads_in.astype(jnp.float32)
    first_half = wide[..., :half_width]
    second_half = wide[..., half_width:]
    joined = jnp.concatenate(
        [
            first_half * cos_part - second_half * sin_part,
            second_half * cos_part + first_half * sin_part,
        ],
        -1,
    )
    return joined.astype(jnp.bfloat16)


ALL = ("gx", "yz")


def spread_rows(inputs, groups):
    rows_here, width = inputs.shape
    block = width // groups
    blocks = inputs.reshape(rows_here, groups, block).transpose(1, 0, 2)
    devices = lax.psum(1, ALL)
    send = jnp.broadcast_to(
        blocks[:, None], (groups, devices // groups, rows_here, block)
    ).reshape(devices, rows_here, block)
    return lax.all_to_all(send, ALL, 0, 0, tiled=True)


def gather_rows(partial, groups, link_type):
    devices, rows_here, width = partial.shape
    got = lax.all_to_all(partial.astype(link_type), ALL, 0, 0, tiled=True)
    summed = jnp.sum(
        got.reshape(groups, devices // groups, rows_here, width).astype(jnp.float32), axis=0
    )
    return summed.transpose(1, 0, 2).reshape(rows_here, (devices // groups) * width)


def project(inputs, weight, link_type=jnp.bfloat16):
    groups = lax.psum(1, "gx")
    spread = spread_rows(inputs, groups)
    partial = jnp.einsum("dsk,kn->dsn", spread, weight, preferred_element_type=jnp.float32)
    return gather_rows(partial, groups, link_type).astype(jnp.bfloat16)


def head_logits(normed, lm_full):
    return jnp.dot(normed, lm_full, preferred_element_type=jnp.float32)


def attend(queries, k_cache, v_cache, lengths, keys_new, values_new):
    groups = HEADS // KV_HEADS
    factor = 1.0 / math.sqrt(HEAD)
    steps = queries.shape[0]
    cache_len = k_cache.shape[1]
    query_heads = queries.reshape(steps, KV_HEADS, groups, HEAD)
    kcache_heads = k_cache.reshape(cache_len, KV_HEADS, HEAD)
    vcache_heads = v_cache.reshape(cache_len, KV_HEADS, HEAD)
    knew_heads = keys_new.reshape(steps, KV_HEADS, HEAD)
    vnew_heads = values_new.reshape(steps, KV_HEADS, HEAD)
    scores_cache = (
        jnp.einsum("skgd,lkd->skgl", query_heads, kcache_heads, preferred_element_type=jnp.float32)
        * factor
    )
    valid = jnp.arange(cache_len)[None, None, None, :] < lengths[0]
    scores_cache = jnp.where(valid, scores_cache, -jnp.inf)
    scores_new = (
        jnp.einsum("skgd,nkd->skgn", query_heads, knew_heads, preferred_element_type=jnp.float32)
        * factor
    )
    causal = (
        jnp.arange(steps)[None, None, None, :] <= jnp.arange(steps)[:, None, None, None]
    )
    scores_new = jnp.where(causal, scores_new, -jnp.inf)
    largest = jnp.maximum(jnp.max(scores_cache, -1), jnp.max(scores_new, -1))[..., None]
    exp_cache = jnp.where(valid, jnp.exp(scores_cache - largest), 0.0)
    exp_new = jnp.where(causal, jnp.exp(scores_new - largest), 0.0)
    denominator = jnp.sum(exp_cache, -1, keepdims=True) + jnp.sum(exp_new, -1, keepdims=True)
    weights_cache = (exp_cache / denominator).astype(jnp.bfloat16)
    weights_new = (exp_new / denominator).astype(jnp.bfloat16)
    result = jnp.einsum(
        "skgl,lkd->skgd", weights_cache, vcache_heads, preferred_element_type=jnp.float32
    )
    result = result + jnp.einsum(
        "skgn,nkd->skgd", weights_new, vnew_heads, preferred_element_type=jnp.float32
    )
    return result.reshape(steps, HEADS * HEAD).astype(jnp.bfloat16)


def element_table(token_elem):
    return (token_elem[:, None] == jnp.arange(ELEMENTS, dtype=jnp.int32)[None, :]).astype(
        jnp.float32
    )


def masked_log_probs(logits, remaining, token_elem):
    element_hot = element_table(token_elem)
    per_token = jnp.dot(remaining, element_hot.T)
    allowed = (per_token > 0.5) | (token_elem == ELEMENTS)[None, :]
    largest = jnp.max(jnp.where(allowed, logits, -jnp.inf), -1, keepdims=True)
    shifted = logits - largest
    denominator = jnp.sum(jnp.where(allowed, jnp.exp(shifted), 0.0), -1, keepdims=True)
    return jnp.where(allowed, shifted - jnp.log(denominator), 0.0)


def used_elements(tokens, token_elem):
    token_hot = (tokens[:, None] == jnp.arange(VOCAB, dtype=jnp.int32)[None, :]).astype(jnp.float32)
    return jnp.dot(token_hot, element_table(token_elem))


def per_device(
    hidden_in,
    k_cache,
    v_cache,
    lengths,
    counts,
    token_elem,
    tokens,
    attn_gain,
    qkv_weight,
    o_weight,
    ffn_gain,
    gate_up_weight,
    down_weight,
    final_gain,
    lm_weight,
):
    q_width = HEADS * HEAD
    kv_width = KV_HEADS * HEAD
    steps = hidden_in.shape[0]
    lm_full = lax.all_gather(lm_weight, ALL, axis=0, tiled=True)
    layer_in = hidden_in[:, 0, :]
    positions = lengths[0] + jnp.arange(steps, dtype=jnp.int32)
    mixed = project(norm_rows(layer_in, attn_gain), qkv_weight)
    queries = rotate(mixed[:, :q_width].reshape(-1, HEADS, HEAD), positions).reshape(-1, q_width)
    keys_now = rotate(
        mixed[:, q_width : q_width + kv_width].reshape(-1, KV_HEADS, HEAD), positions
    ).reshape(-1, kv_width)
    values_now = mixed[:, q_width + kv_width :]
    attended = attend(queries, k_cache[0], v_cache[0], lengths, keys_now, values_now)
    projected = project(attended, o_weight)
    residual = (layer_in.astype(jnp.float32) + projected.astype(jnp.float32)).astype(jnp.bfloat16)
    gate_up = project(norm_rows(residual, ffn_gain), gate_up_weight)
    hidden_units = (
        jax.nn.silu(gate_up[:, :FF].astype(jnp.float32)) * gate_up[:, FF:].astype(jnp.float32)
    ).astype(jnp.bfloat16)
    lowered = project(hidden_units, down_weight)
    result = (residual.astype(jnp.float32) + lowered.astype(jnp.float32)).astype(jnp.bfloat16)
    logits = head_logits(norm_rows(result, final_gain), lm_full)
    remaining = counts.astype(jnp.float32)
    first_log = masked_log_probs(logits[0:1], remaining, token_elem)
    remaining = remaining - used_elements(tokens, token_elem)
    second_log = masked_log_probs(logits[1:2], remaining, token_elem)
    return (result[:, None, :], jnp.stack([first_log, second_log]))


def solution(mesh):
    return jax.shard_map(
        per_device,
        mesh=mesh,
        in_specs=(
            P(None, ("gx", "yz"), None),
            P(("gx", "yz"), None, None),
            P(("gx", "yz"), None, None),
            P(("gx", "yz")),
            P(("gx", "yz"), None),
            P(),
            P(("gx", "yz")),
            P(),
            P("gx", "yz"),
            P("gx", "yz"),
            P(),
            P("gx", "yz"),
            P("gx", "yz"),
            P(),
            P(("gx", "yz"), None),
        ),
        out_specs=(P(None, ("gx", "yz"), None), P(None, ("gx", "yz"), None)),
        check_vma=False,
    )
```

```python
import math

import jax
import jax.numpy as jnp
from jax import lax
from jax.sharding import PartitionSpec as P

FF = 28672
HEADS = 64
KV_HEADS = 8
HEAD = 128
VOCAB = 512
ELEMENTS = 16


NORM_EPS = 1e-05
ROPE_THETA = 500000.0


def norm_rows(values, gain_vec):
    wide = values.astype(jnp.float32)
    inverse = lax.rsqrt(jnp.mean(wide * wide, axis=-1, keepdims=True) + NORM_EPS)
    return (wide * inverse * gain_vec).astype(jnp.bfloat16)


def rotate(heads_in, positions):
    half_width = heads_in.shape[-1] // 2
    frequency = jnp.power(
        ROPE_THETA, -(jnp.arange(half_width, dtype=jnp.float32) * 2.0 / heads_in.shape[-1])
    )
    angles = positions.astype(jnp.float32)[:, None] * frequency[None, :]
    cos_part = jnp.cos(angles)[:, None, :]
    sin_part = jnp.sin(angles)[:, None, :]
    wide = heads_in.astype(jnp.float32)
    first_half = wide[..., :half_width]
    second_half = wide[..., half_width:]
    joined = jnp.concatenate(
        [
            first_half * cos_part - second_half * sin_part,
            second_half * cos_part + first_half * sin_part,
        ],
        -1,
    )
    return joined.astype(jnp.bfloat16)


ALL = ("gx", "yz")


def spread_rows(inputs, groups):
    rows_here, width = inputs.shape
    block = width // groups
    blocks = inputs.reshape(rows_here, groups, block).transpose(1, 0, 2)
    devices = lax.psum(1, ALL)
    send = jnp.broadcast_to(
        blocks[:, None], (groups, devices // groups, rows_here, block)
    ).reshape(devices, rows_here, block)
    return lax.all_to_all(send, ALL, 0, 0, tiled=True)


def gather_rows(partial, groups, link_type):
    devices, rows_here, width = partial.shape
    got = lax.all_to_all(partial.astype(link_type), ALL, 0, 0, tiled=True)
    summed = jnp.sum(
        got.reshape(groups, devices // groups, rows_here, width).astype(jnp.float32), axis=0
    )
    return summed.transpose(1, 0, 2).reshape(rows_here, (devices // groups) * width)


def project(inputs, weight, link_type=jnp.bfloat16):
    groups = lax.psum(1, "gx")
    spread = spread_rows(inputs, groups)
    partial = jnp.einsum("dsk,kn->dsn", spread, weight, preferred_element_type=jnp.float32)
    return gather_rows(partial, groups, link_type).astype(jnp.bfloat16)


SHIFT_ORDER = (2, 8, 64, 32, 4, 1, 16)


def gather_weight(shard):
    devices = lax.psum(1, ALL)
    held = shard
    for step in SHIFT_ORDER:
        pairs = [(i, i ^ step) for i in range(devices)]
        held = jnp.concatenate([held, lax.ppermute(held, ALL, pairs)], axis=0)
    return held


def held_order():
    return [
        sum(step for bit, step in enumerate(SHIFT_ORDER) if (place >> bit) & 1)
        for place in range(2 ** len(SHIFT_ORDER))
    ]


def head_logits(normed, lm_held):
    devices = lax.psum(1, ALL)
    me = lax.axis_index(ALL)
    rows_here, width = normed.shape
    order = jnp.bitwise_xor(me, jnp.array(held_order(), dtype=jnp.int32))
    matched = jnp.take(normed.reshape(rows_here, devices, width // devices), order, axis=1)
    return jnp.dot(matched.reshape(rows_here, width), lm_held, preferred_element_type=jnp.float32)


def attend(queries, k_cache, v_cache, lengths, keys_new, values_new):
    groups = HEADS // KV_HEADS
    factor = 1.0 / math.sqrt(HEAD)
    steps = queries.shape[0]
    cache_len = k_cache.shape[1]
    query_heads = queries.reshape(steps, KV_HEADS, groups, HEAD)
    kcache_heads = k_cache.reshape(cache_len, KV_HEADS, HEAD)
    vcache_heads = v_cache.reshape(cache_len, KV_HEADS, HEAD)
    knew_heads = keys_new.reshape(steps, KV_HEADS, HEAD)
    vnew_heads = values_new.reshape(steps, KV_HEADS, HEAD)
    scores_cache = (
        jnp.einsum("skgd,lkd->skgl", query_heads, kcache_heads, preferred_element_type=jnp.float32)
        * factor
    )
    valid = jnp.arange(cache_len)[None, None, None, :] < lengths[0]
    scores_cache = jnp.where(valid, scores_cache, -jnp.inf)
    scores_new = (
        jnp.einsum("skgd,nkd->skgn", query_heads, knew_heads, preferred_element_type=jnp.float32)
        * factor
    )
    causal = (
        jnp.arange(steps)[None, None, None, :] <= jnp.arange(steps)[:, None, None, None]
    )
    scores_new = jnp.where(causal, scores_new, -jnp.inf)
    largest = jnp.maximum(jnp.max(scores_cache, -1), jnp.max(scores_new, -1))[..., None]
    exp_cache = jnp.where(valid, jnp.exp(scores_cache - largest), 0.0)
    exp_new = jnp.where(causal, jnp.exp(scores_new - largest), 0.0)
    denominator = jnp.sum(exp_cache, -1, keepdims=True) + jnp.sum(exp_new, -1, keepdims=True)
    weights_cache = (exp_cache / denominator).astype(jnp.bfloat16)
    weights_new = (exp_new / denominator).astype(jnp.bfloat16)
    result = jnp.einsum(
        "skgl,lkd->skgd", weights_cache, vcache_heads, preferred_element_type=jnp.float32
    )
    result = result + jnp.einsum(
        "skgn,nkd->skgd", weights_new, vnew_heads, preferred_element_type=jnp.float32
    )
    return result.reshape(steps, HEADS * HEAD).astype(jnp.bfloat16)


def element_table(token_elem):
    return (token_elem[:, None] == jnp.arange(ELEMENTS, dtype=jnp.int32)[None, :]).astype(
        jnp.float32
    )


def masked_log_probs(logits, remaining, token_elem):
    element_hot = element_table(token_elem)
    per_token = jnp.dot(remaining, element_hot.T)
    allowed = (per_token > 0.5) | (token_elem == ELEMENTS)[None, :]
    largest = jnp.max(jnp.where(allowed, logits, -jnp.inf), -1, keepdims=True)
    shifted = logits - largest
    denominator = jnp.sum(jnp.where(allowed, jnp.exp(shifted), 0.0), -1, keepdims=True)
    return jnp.where(allowed, shifted - jnp.log(denominator), 0.0)


def used_elements(tokens, token_elem):
    token_hot = (tokens[:, None] == jnp.arange(VOCAB, dtype=jnp.int32)[None, :]).astype(jnp.float32)
    return jnp.dot(token_hot, element_table(token_elem))


def per_device(
    hidden_in,
    k_cache,
    v_cache,
    lengths,
    counts,
    token_elem,
    tokens,
    attn_gain,
    qkv_weight,
    o_weight,
    ffn_gain,
    gate_up_weight,
    down_weight,
    final_gain,
    lm_weight,
):
    q_width = HEADS * HEAD
    kv_width = KV_HEADS * HEAD
    steps = hidden_in.shape[0]
    lm_full = gather_weight(lm_weight)
    layer_in = hidden_in[:, 0, :]
    positions = lengths[0] + jnp.arange(steps, dtype=jnp.int32)
    mixed = project(norm_rows(layer_in, attn_gain), qkv_weight)
    queries = rotate(mixed[:, :q_width].reshape(-1, HEADS, HEAD), positions).reshape(-1, q_width)
    keys_now = rotate(
        mixed[:, q_width : q_width + kv_width].reshape(-1, KV_HEADS, HEAD), positions
    ).reshape(-1, kv_width)
    values_now = mixed[:, q_width + kv_width :]
    attended = attend(queries, k_cache[0], v_cache[0], lengths, keys_now, values_now)
    projected = project(attended, o_weight)
    residual = (layer_in.astype(jnp.float32) + projected.astype(jnp.float32)).astype(jnp.bfloat16)
    gate_up = project(norm_rows(residual, ffn_gain), gate_up_weight)
    hidden_units = (
        jax.nn.silu(gate_up[:, :FF].astype(jnp.float32)) * gate_up[:, FF:].astype(jnp.float32)
    ).astype(jnp.bfloat16)
    lowered = project(hidden_units, down_weight)
    result = (residual.astype(jnp.float32) + lowered.astype(jnp.float32)).astype(jnp.bfloat16)
    logits = head_logits(norm_rows(result, final_gain), lm_full)
    remaining = counts.astype(jnp.float32)
    first_log = masked_log_probs(logits[0:1], remaining, token_elem)
    remaining = remaining - used_elements(tokens, token_elem)
    second_log = masked_log_probs(logits[1:2], remaining, token_elem)
    return (result[:, None, :], jnp.stack([first_log, second_log]))


def solution(mesh):
    return jax.shard_map(
        per_device,
        mesh=mesh,
        in_specs=(
            P(None, ("gx", "yz"), None),
            P(("gx", "yz"), None, None),
            P(("gx", "yz"), None, None),
            P(("gx", "yz")),
            P(("gx", "yz"), None),
            P(),
            P(("gx", "yz")),
            P(),
            P("gx", "yz"),
            P("gx", "yz"),
            P(),
            P("gx", "yz"),
            P("gx", "yz"),
            P(),
            P(("gx", "yz"), None),
        ),
        out_specs=(P(None, ("gx", "yz"), None), P(None, ("gx", "yz"), None)),
        check_vma=False,
    )
```

```python
import math

import jax
import jax.numpy as jnp
from jax import lax
from jax.sharding import PartitionSpec as P

FF = 28672
HEADS = 64
KV_HEADS = 8
HEAD = 128
VOCAB = 512
ELEMENTS = 16


NORM_EPS = 1e-05
ROPE_THETA = 500000.0


def norm_rows(values, gain_vec):
    wide = values.astype(jnp.float32)
    inverse = lax.rsqrt(jnp.mean(wide * wide, axis=-1, keepdims=True) + NORM_EPS)
    return (wide * inverse * gain_vec).astype(jnp.bfloat16)


def rotate(heads_in, positions):
    half_width = heads_in.shape[-1] // 2
    frequency = jnp.power(
        ROPE_THETA, -(jnp.arange(half_width, dtype=jnp.float32) * 2.0 / heads_in.shape[-1])
    )
    angles = positions.astype(jnp.float32)[:, None] * frequency[None, :]
    cos_part = jnp.cos(angles)[:, None, :]
    sin_part = jnp.sin(angles)[:, None, :]
    wide = heads_in.astype(jnp.float32)
    first_half = wide[..., :half_width]
    second_half = wide[..., half_width:]
    joined = jnp.concatenate(
        [
            first_half * cos_part - second_half * sin_part,
            second_half * cos_part + first_half * sin_part,
        ],
        -1,
    )
    return joined.astype(jnp.bfloat16)


ALL = ("gx", "yz")


def spread_rows(inputs, groups):
    rows_here, width = inputs.shape
    block = width // groups
    blocks = inputs.reshape(rows_here, groups, block).transpose(1, 0, 2)
    devices = lax.psum(1, ALL)
    send = jnp.broadcast_to(
        blocks[:, None], (groups, devices // groups, rows_here, block)
    ).reshape(devices, rows_here, block)
    return lax.all_to_all(send, ALL, 0, 0, tiled=True)


def gather_rows(partial, groups, link_type):
    devices, rows_here, width = partial.shape
    got = lax.all_to_all(partial.astype(link_type), ALL, 0, 0, tiled=True)
    summed = jnp.sum(
        got.reshape(groups, devices // groups, rows_here, width).astype(jnp.float32), axis=0
    )
    return summed.transpose(1, 0, 2).reshape(rows_here, (devices // groups) * width)


def project(inputs, weight, tie_in, tie_out, link_type=jnp.bfloat16):
    groups = lax.psum(1, "gx")
    spread = spread_rows(tie_in(inputs), groups)
    partial = jnp.einsum("dsk,kn->dsn", spread, weight, preferred_element_type=jnp.float32)
    return gather_rows(tie_out(partial), groups, link_type).astype(jnp.bfloat16)


SHIFT_ORDER = (2, 8, 64, 32, 4, 1, 16)


class WeightGather:
    def __init__(self, shard):
        self.held = shard
        self.done = 0

    def tie(self, value):
        if self.done == len(SHIFT_ORDER):
            return value
        devices = lax.psum(1, ALL)
        step = SHIFT_ORDER[self.done]
        pairs = [(i, i ^ step) for i in range(devices)]
        grown = jnp.concatenate([self.held, lax.ppermute(self.held, ALL, pairs)], axis=0)
        self.held, value = lax.optimization_barrier((grown, value))
        self.done += 1
        return value

    def result(self):
        while self.done < len(SHIFT_ORDER):
            self.tie(jnp.zeros((), jnp.float32))
        return self.held


def held_order():
    return [
        sum(step for bit, step in enumerate(SHIFT_ORDER) if (place >> bit) & 1)
        for place in range(2 ** len(SHIFT_ORDER))
    ]


def head_logits(normed, lm_held):
    devices = lax.psum(1, ALL)
    me = lax.axis_index(ALL)
    rows_here, width = normed.shape
    order = jnp.bitwise_xor(me, jnp.array(held_order(), dtype=jnp.int32))
    matched = jnp.take(normed.reshape(rows_here, devices, width // devices), order, axis=1)
    return jnp.dot(matched.reshape(rows_here, width), lm_held, preferred_element_type=jnp.float32)


def attend(queries, k_cache, v_cache, lengths, keys_new, values_new):
    groups = HEADS // KV_HEADS
    factor = 1.0 / math.sqrt(HEAD)
    steps = queries.shape[0]
    cache_len = k_cache.shape[1]
    query_heads = queries.reshape(steps, KV_HEADS, groups, HEAD)
    kcache_heads = k_cache.reshape(cache_len, KV_HEADS, HEAD)
    vcache_heads = v_cache.reshape(cache_len, KV_HEADS, HEAD)
    knew_heads = keys_new.reshape(steps, KV_HEADS, HEAD)
    vnew_heads = values_new.reshape(steps, KV_HEADS, HEAD)
    scores_cache = (
        jnp.einsum("skgd,lkd->skgl", query_heads, kcache_heads, preferred_element_type=jnp.float32)
        * factor
    )
    valid = jnp.arange(cache_len)[None, None, None, :] < lengths[0]
    scores_cache = jnp.where(valid, scores_cache, -jnp.inf)
    scores_new = (
        jnp.einsum("skgd,nkd->skgn", query_heads, knew_heads, preferred_element_type=jnp.float32)
        * factor
    )
    causal = (
        jnp.arange(steps)[None, None, None, :] <= jnp.arange(steps)[:, None, None, None]
    )
    scores_new = jnp.where(causal, scores_new, -jnp.inf)
    largest = jnp.maximum(jnp.max(scores_cache, -1), jnp.max(scores_new, -1))[..., None]
    exp_cache = jnp.where(valid, jnp.exp(scores_cache - largest), 0.0)
    exp_new = jnp.where(causal, jnp.exp(scores_new - largest), 0.0)
    denominator = jnp.sum(exp_cache, -1, keepdims=True) + jnp.sum(exp_new, -1, keepdims=True)
    weights_cache = (exp_cache / denominator).astype(jnp.bfloat16)
    weights_new = (exp_new / denominator).astype(jnp.bfloat16)
    result = jnp.einsum(
        "skgl,lkd->skgd", weights_cache, vcache_heads, preferred_element_type=jnp.float32
    )
    result = result + jnp.einsum(
        "skgn,nkd->skgd", weights_new, vnew_heads, preferred_element_type=jnp.float32
    )
    return result.reshape(steps, HEADS * HEAD).astype(jnp.bfloat16)


def element_table(token_elem):
    return (token_elem[:, None] == jnp.arange(ELEMENTS, dtype=jnp.int32)[None, :]).astype(
        jnp.float32
    )


def masked_log_probs(logits, remaining, token_elem):
    element_hot = element_table(token_elem)
    per_token = jnp.dot(remaining, element_hot.T)
    allowed = (per_token > 0.5) | (token_elem == ELEMENTS)[None, :]
    largest = jnp.max(jnp.where(allowed, logits, -jnp.inf), -1, keepdims=True)
    shifted = logits - largest
    denominator = jnp.sum(jnp.where(allowed, jnp.exp(shifted), 0.0), -1, keepdims=True)
    return jnp.where(allowed, shifted - jnp.log(denominator), 0.0)


def used_elements(tokens, token_elem):
    token_hot = (tokens[:, None] == jnp.arange(VOCAB, dtype=jnp.int32)[None, :]).astype(jnp.float32)
    return jnp.dot(token_hot, element_table(token_elem))


def per_device(
    hidden_in,
    k_cache,
    v_cache,
    lengths,
    counts,
    token_elem,
    tokens,
    attn_gain,
    qkv_weight,
    o_weight,
    ffn_gain,
    gate_up_weight,
    down_weight,
    final_gain,
    lm_weight,
):
    q_width = HEADS * HEAD
    kv_width = KV_HEADS * HEAD
    steps = hidden_in.shape[0]
    lm_gather = WeightGather(lm_weight)
    tie = lm_gather.tie

    def keep(value):
        return value

    layer_in = hidden_in[:, 0, :]
    positions = lengths[0] + jnp.arange(steps, dtype=jnp.int32)
    mixed = project(norm_rows(layer_in, attn_gain), qkv_weight, keep, tie)
    queries = rotate(mixed[:, :q_width].reshape(-1, HEADS, HEAD), positions).reshape(-1, q_width)
    keys_now = rotate(
        mixed[:, q_width : q_width + kv_width].reshape(-1, KV_HEADS, HEAD), positions
    ).reshape(-1, kv_width)
    values_now = mixed[:, q_width + kv_width :]
    attended = attend(queries, k_cache[0], v_cache[0], lengths, keys_now, values_now)
    projected = project(attended, o_weight, tie, tie)
    residual = (layer_in.astype(jnp.float32) + projected.astype(jnp.float32)).astype(jnp.bfloat16)
    gate_up = project(norm_rows(residual, ffn_gain), gate_up_weight, tie, tie)
    hidden_units = (
        jax.nn.silu(gate_up[:, :FF].astype(jnp.float32)) * gate_up[:, FF:].astype(jnp.float32)
    ).astype(jnp.bfloat16)
    lowered = project(hidden_units, down_weight, tie, tie)
    result = (residual.astype(jnp.float32) + lowered.astype(jnp.float32)).astype(jnp.bfloat16)
    logits = head_logits(norm_rows(result, final_gain), lm_gather.result())
    remaining = counts.astype(jnp.float32)
    first_log = masked_log_probs(logits[0:1], remaining, token_elem)
    remaining = remaining - used_elements(tokens, token_elem)
    second_log = masked_log_probs(logits[1:2], remaining, token_elem)
    return (result[:, None, :], jnp.stack([first_log, second_log]))


def solution(mesh):
    return jax.shard_map(
        per_device,
        mesh=mesh,
        in_specs=(
            P(None, ("gx", "yz"), None),
            P(("gx", "yz"), None, None),
            P(("gx", "yz"), None, None),
            P(("gx", "yz")),
            P(("gx", "yz"), None),
            P(),
            P(("gx", "yz")),
            P(),
            P("gx", "yz"),
            P("gx", "yz"),
            P(),
            P("gx", "yz"),
            P("gx", "yz"),
            P(),
            P(("gx", "yz"), None),
        ),
        out_specs=(P(None, ("gx", "yz"), None), P(None, ("gx", "yz"), None)),
        check_vma=False,
    )
```

```python
import math

import jax
import jax.numpy as jnp
from jax import lax
from jax.sharding import PartitionSpec as P

FF = 28672
HEADS = 64
KV_HEADS = 8
HEAD = 128
VOCAB = 512
ELEMENTS = 16


NORM_EPS = 1e-05
ROPE_THETA = 500000.0


def norm_rows(values, gain_vec):
    wide = values.astype(jnp.float32)
    inverse = lax.rsqrt(jnp.mean(wide * wide, axis=-1, keepdims=True) + NORM_EPS)
    return (wide * inverse * gain_vec).astype(jnp.bfloat16)


def rotate(heads_in, positions):
    half_width = heads_in.shape[-1] // 2
    frequency = jnp.power(
        ROPE_THETA, -(jnp.arange(half_width, dtype=jnp.float32) * 2.0 / heads_in.shape[-1])
    )
    angles = positions.astype(jnp.float32)[:, None] * frequency[None, :]
    cos_part = jnp.cos(angles)[:, None, :]
    sin_part = jnp.sin(angles)[:, None, :]
    wide = heads_in.astype(jnp.float32)
    first_half = wide[..., :half_width]
    second_half = wide[..., half_width:]
    joined = jnp.concatenate(
        [
            first_half * cos_part - second_half * sin_part,
            second_half * cos_part + first_half * sin_part,
        ],
        -1,
    )
    return joined.astype(jnp.bfloat16)


ALL = ("gx", "yz")


def spread_rows(inputs, groups):
    rows_here, width = inputs.shape
    block = width // groups
    blocks = jnp.stack([inputs[:, g * block : (g + 1) * block] for g in range(groups)])
    devices = lax.psum(1, ALL)
    send = jnp.broadcast_to(
        blocks[:, None], (groups, devices // groups, rows_here, block)
    ).reshape(devices, rows_here, block)
    return lax.all_to_all(send, ALL, 0, 0, tiled=True)


def gather_rows(partial, groups, link_type):
    devices, rows_here, width = partial.shape
    got = lax.all_to_all(partial.astype(link_type), ALL, 0, 0, tiled=True)
    summed = jnp.sum(
        got.reshape(groups, devices // groups, rows_here, width).astype(jnp.float32), axis=0
    )
    return summed.transpose(1, 0, 2).reshape(rows_here, (devices // groups) * width)


def project(inputs, weight, link_type=jnp.bfloat16):
    groups = lax.psum(1, "gx")
    spread = spread_rows(inputs, groups)
    partial = jnp.einsum("dsk,kn->dsn", spread, weight, preferred_element_type=jnp.float32)
    return gather_rows(partial, groups, link_type).astype(jnp.bfloat16)


def head_logits(normed, lm_full):
    return jnp.dot(normed, lm_full, preferred_element_type=jnp.float32)


def attend(queries, k_cache, v_cache, lengths, keys_new, values_new):
    groups = HEADS // KV_HEADS
    factor = 1.0 / math.sqrt(HEAD)
    steps = queries.shape[0]
    cache_len = k_cache.shape[1]
    query_heads = queries.reshape(steps, KV_HEADS, groups, HEAD)
    kcache_heads = k_cache.reshape(cache_len, KV_HEADS, HEAD)
    vcache_heads = v_cache.reshape(cache_len, KV_HEADS, HEAD)
    knew_heads = keys_new.reshape(steps, KV_HEADS, HEAD)
    vnew_heads = values_new.reshape(steps, KV_HEADS, HEAD)
    scores_cache = (
        jnp.einsum("skgd,lkd->skgl", query_heads, kcache_heads, preferred_element_type=jnp.float32)
        * factor
    )
    valid = jnp.arange(cache_len)[None, None, None, :] < lengths[0]
    scores_cache = jnp.where(valid, scores_cache, -jnp.inf)
    scores_new = (
        jnp.einsum("skgd,nkd->skgn", query_heads, knew_heads, preferred_element_type=jnp.float32)
        * factor
    )
    causal = (
        jnp.arange(steps)[None, None, None, :] <= jnp.arange(steps)[:, None, None, None]
    )
    scores_new = jnp.where(causal, scores_new, -jnp.inf)
    largest = jnp.maximum(jnp.max(scores_cache, -1), jnp.max(scores_new, -1))[..., None]
    exp_cache = jnp.where(valid, jnp.exp(scores_cache - largest), 0.0)
    exp_new = jnp.where(causal, jnp.exp(scores_new - largest), 0.0)
    denominator = jnp.sum(exp_cache, -1, keepdims=True) + jnp.sum(exp_new, -1, keepdims=True)
    weights_cache = (exp_cache / denominator).astype(jnp.bfloat16)
    weights_new = (exp_new / denominator).astype(jnp.bfloat16)
    result = jnp.einsum(
        "skgl,lkd->skgd", weights_cache, vcache_heads, preferred_element_type=jnp.float32
    )
    result = result + jnp.einsum(
        "skgn,nkd->skgd", weights_new, vnew_heads, preferred_element_type=jnp.float32
    )
    return result.reshape(steps, HEADS * HEAD).astype(jnp.bfloat16)


def allowed_tokens(remaining, token_elem):
    elements = remaining.shape[-1]
    has_element = token_elem < elements
    picked = jnp.take(remaining, jnp.minimum(token_elem, elements - 1), axis=1)
    return (picked > 0.5) & has_element[None, :] | (token_elem == ELEMENTS)[None, :]


def masked_log_probs(logits, allowed):
    largest = jnp.max(jnp.where(allowed, logits, -jnp.inf), -1, keepdims=True)
    shifted = logits - largest
    denominator = jnp.sum(jnp.where(allowed, jnp.exp(shifted), 0.0), -1, keepdims=True)
    return jnp.where(allowed, shifted - jnp.log(denominator), 0.0)


def per_device(
    hidden_in,
    k_cache,
    v_cache,
    lengths,
    counts,
    token_elem,
    tokens,
    attn_gain,
    qkv_weight,
    o_weight,
    ffn_gain,
    gate_up_weight,
    down_weight,
    final_gain,
    lm_weight,
):
    q_width = HEADS * HEAD
    kv_width = KV_HEADS * HEAD
    steps = hidden_in.shape[0]
    lm_full = lax.all_gather(lm_weight, ALL, axis=0, tiled=True)
    layer_in = hidden_in[:, 0, :]
    positions = lengths[0] + jnp.arange(steps, dtype=jnp.int32)
    mixed = project(norm_rows(layer_in, attn_gain), qkv_weight)
    queries = rotate(mixed[:, :q_width].reshape(-1, HEADS, HEAD), positions).reshape(-1, q_width)
    keys_now = rotate(
        mixed[:, q_width : q_width + kv_width].reshape(-1, KV_HEADS, HEAD), positions
    ).reshape(-1, kv_width)
    values_now = mixed[:, q_width + kv_width :]
    attended = attend(queries, k_cache[0], v_cache[0], lengths, keys_now, values_now)
    projected = project(attended, o_weight)
    residual = (layer_in.astype(jnp.float32) + projected.astype(jnp.float32)).astype(jnp.bfloat16)
    gate_up = project(norm_rows(residual, ffn_gain), gate_up_weight)
    hidden_units = (
        jax.nn.silu(gate_up[:, :FF].astype(jnp.float32)) * gate_up[:, FF:].astype(jnp.float32)
    ).astype(jnp.bfloat16)
    lowered = project(hidden_units, down_weight)
    result = (residual.astype(jnp.float32) + lowered.astype(jnp.float32)).astype(jnp.bfloat16)
    logits = head_logits(norm_rows(result, final_gain), lm_full)
    start_counts = counts.astype(jnp.float32)
    used = (jnp.arange(ELEMENTS, dtype=jnp.int32)[None, :] == token_elem[tokens][:, None]).astype(
        jnp.float32
    )
    remaining = jnp.concatenate([start_counts, start_counts - used], axis=0)
    log_probs = masked_log_probs(logits, allowed_tokens(remaining, token_elem))
    return (result[:, None, :], log_probs[:, None, :])


def solution(mesh):
    return jax.shard_map(
        per_device,
        mesh=mesh,
        in_specs=(
            P(None, ("gx", "yz"), None),
            P(("gx", "yz"), None, None),
            P(("gx", "yz"), None, None),
            P(("gx", "yz")),
            P(("gx", "yz"), None),
            P(),
            P(("gx", "yz")),
            P(),
            P("gx", "yz"),
            P("gx", "yz"),
            P(),
            P("gx", "yz"),
            P("gx", "yz"),
            P(),
            P(("gx", "yz"), None),
        ),
        out_specs=(P(None, ("gx", "yz"), None), P(None, ("gx", "yz"), None)),
        check_vma=False,
    )
```

```python
import math

import jax
import jax.numpy as jnp
from jax import lax
from jax.sharding import PartitionSpec as P

FF = 28672
HEADS = 64
KV_HEADS = 8
HEAD = 128
VOCAB = 512
ELEMENTS = 16


NORM_EPS = 1e-05
ROPE_THETA = 500000.0


def norm_rows(values, gain_vec):
    wide = values.astype(jnp.float32)
    inverse = lax.rsqrt(jnp.mean(wide * wide, axis=-1, keepdims=True) + NORM_EPS)
    return (wide * inverse * gain_vec).astype(jnp.bfloat16)


def rotate(heads_in, positions):
    half_width = heads_in.shape[-1] // 2
    frequency = jnp.power(
        ROPE_THETA, -(jnp.arange(half_width, dtype=jnp.float32) * 2.0 / heads_in.shape[-1])
    )
    angles = positions.astype(jnp.float32)[:, None] * frequency[None, :]
    cos_part = jnp.cos(angles)[:, None, :]
    sin_part = jnp.sin(angles)[:, None, :]
    wide = heads_in.astype(jnp.float32)
    first_half = wide[..., :half_width]
    second_half = wide[..., half_width:]
    joined = jnp.concatenate(
        [
            first_half * cos_part - second_half * sin_part,
            second_half * cos_part + first_half * sin_part,
        ],
        -1,
    )
    return joined.astype(jnp.bfloat16)


ALL = ("gx", "yz")


def spread_rows(inputs, groups, sliced=False):
    rows_here, width = inputs.shape
    block = width // groups
    if sliced:
        blocks = jnp.stack([inputs[:, g * block : (g + 1) * block] for g in range(groups)])
    else:
        blocks = inputs.reshape(rows_here, groups, block).transpose(1, 0, 2)
    devices = lax.psum(1, ALL)
    send = jnp.broadcast_to(
        blocks[:, None], (groups, devices // groups, rows_here, block)
    ).reshape(devices, rows_here, block)
    return lax.all_to_all(send, ALL, 0, 0, tiled=True)


def gather_rows(partial, groups, link_type):
    devices, rows_here, width = partial.shape
    got = lax.all_to_all(partial.astype(link_type), ALL, 0, 0, tiled=True)
    summed = jnp.sum(
        got.reshape(groups, devices // groups, rows_here, width).astype(jnp.float32), axis=0
    )
    return summed.transpose(1, 0, 2).reshape(rows_here, (devices // groups) * width)


def project(inputs, weight, link_type=jnp.bfloat16, sliced=False):
    groups = lax.psum(1, "gx")
    spread = spread_rows(inputs, groups, sliced)
    partial = jnp.einsum("dsk,kn->dsn", spread, weight, preferred_element_type=jnp.float32)
    return gather_rows(partial, groups, link_type).astype(jnp.bfloat16)


def head_logits(normed, lm_full):
    return jnp.dot(normed, lm_full, preferred_element_type=jnp.float32)


def attend(queries, k_cache, v_cache, lengths, keys_new, values_new):
    groups = HEADS // KV_HEADS
    factor = 1.0 / math.sqrt(HEAD)
    steps = queries.shape[0]
    cache_len = k_cache.shape[1]
    query_heads = queries.reshape(steps, KV_HEADS, groups, HEAD)
    kcache_heads = k_cache.reshape(cache_len, KV_HEADS, HEAD)
    vcache_heads = v_cache.reshape(cache_len, KV_HEADS, HEAD)
    knew_heads = keys_new.reshape(steps, KV_HEADS, HEAD)
    vnew_heads = values_new.reshape(steps, KV_HEADS, HEAD)
    scores_cache = (
        jnp.einsum("skgd,lkd->skgl", query_heads, kcache_heads, preferred_element_type=jnp.float32)
        * factor
    )
    valid = jnp.arange(cache_len)[None, None, None, :] < lengths[0]
    scores_cache = jnp.where(valid, scores_cache, -jnp.inf)
    scores_new = (
        jnp.einsum("skgd,nkd->skgn", query_heads, knew_heads, preferred_element_type=jnp.float32)
        * factor
    )
    causal = (
        jnp.arange(steps)[None, None, None, :] <= jnp.arange(steps)[:, None, None, None]
    )
    scores_new = jnp.where(causal, scores_new, -jnp.inf)
    largest = jnp.maximum(jnp.max(scores_cache, -1), jnp.max(scores_new, -1))[..., None]
    exp_cache = jnp.where(valid, jnp.exp(scores_cache - largest), 0.0)
    exp_new = jnp.where(causal, jnp.exp(scores_new - largest), 0.0)
    denominator = jnp.sum(exp_cache, -1, keepdims=True) + jnp.sum(exp_new, -1, keepdims=True)
    weights_cache = (exp_cache / denominator).astype(jnp.bfloat16)
    weights_new = (exp_new / denominator).astype(jnp.bfloat16)
    result = jnp.einsum(
        "skgl,lkd->skgd", weights_cache, vcache_heads, preferred_element_type=jnp.float32
    )
    result = result + jnp.einsum(
        "skgn,nkd->skgd", weights_new, vnew_heads, preferred_element_type=jnp.float32
    )
    return result.reshape(steps, HEADS * HEAD).astype(jnp.bfloat16)


def allowed_tokens(remaining, token_elem):
    elements = remaining.shape[-1]
    has_element = token_elem < elements
    picked = jnp.take(remaining, jnp.minimum(token_elem, elements - 1), axis=1)
    return (picked > 0.5) & has_element[None, :] | (token_elem == ELEMENTS)[None, :]


def masked_log_probs(logits, allowed):
    largest = jnp.max(jnp.where(allowed, logits, -jnp.inf), -1, keepdims=True)
    shifted = logits - largest
    denominator = jnp.sum(jnp.where(allowed, jnp.exp(shifted), 0.0), -1, keepdims=True)
    return jnp.where(allowed, shifted - jnp.log(denominator), 0.0)


def per_device(
    hidden_in,
    k_cache,
    v_cache,
    lengths,
    counts,
    token_elem,
    tokens,
    attn_gain,
    qkv_weight,
    o_weight,
    ffn_gain,
    gate_up_weight,
    down_weight,
    final_gain,
    lm_weight,
):
    q_width = HEADS * HEAD
    kv_width = KV_HEADS * HEAD
    steps = hidden_in.shape[0]
    lm_full = lax.all_gather(lm_weight, ALL, axis=0, tiled=True)
    layer_in = hidden_in[:, 0, :]
    positions = lengths[0] + jnp.arange(steps, dtype=jnp.int32)
    mixed = project(norm_rows(layer_in, attn_gain), qkv_weight, sliced=True)
    queries = rotate(mixed[:, :q_width].reshape(-1, HEADS, HEAD), positions).reshape(-1, q_width)
    keys_now = rotate(
        mixed[:, q_width : q_width + kv_width].reshape(-1, KV_HEADS, HEAD), positions
    ).reshape(-1, kv_width)
    values_now = mixed[:, q_width + kv_width :]
    attended = attend(queries, k_cache[0], v_cache[0], lengths, keys_now, values_now)
    projected = project(attended, o_weight)
    residual = (layer_in.astype(jnp.float32) + projected.astype(jnp.float32)).astype(jnp.bfloat16)
    gate_up = project(norm_rows(residual, ffn_gain), gate_up_weight)
    hidden_units = (
        jax.nn.silu(gate_up[:, :FF].astype(jnp.float32)) * gate_up[:, FF:].astype(jnp.float32)
    ).astype(jnp.bfloat16)
    lowered = project(hidden_units, down_weight)
    result = (residual.astype(jnp.float32) + lowered.astype(jnp.float32)).astype(jnp.bfloat16)
    logits = head_logits(norm_rows(result, final_gain), lm_full)
    start_counts = counts.astype(jnp.float32)
    used = (jnp.arange(ELEMENTS, dtype=jnp.int32)[None, :] == token_elem[tokens][:, None]).astype(
        jnp.float32
    )
    remaining = jnp.concatenate([start_counts, start_counts - used], axis=0)
    log_probs = masked_log_probs(logits, allowed_tokens(remaining, token_elem))
    return (result[:, None, :], log_probs[:, None, :])


def solution(mesh):
    return jax.shard_map(
        per_device,
        mesh=mesh,
        in_specs=(
            P(None, ("gx", "yz"), None),
            P(("gx", "yz"), None, None),
            P(("gx", "yz"), None, None),
            P(("gx", "yz")),
            P(("gx", "yz"), None),
            P(),
            P(("gx", "yz")),
            P(),
            P("gx", "yz"),
            P("gx", "yz"),
            P(),
            P("gx", "yz"),
            P("gx", "yz"),
            P(),
            P(("gx", "yz"), None),
        ),
        out_specs=(P(None, ("gx", "yz"), None), P(None, ("gx", "yz"), None)),
        check_vma=False,
    )
```
